1024 devices in a mesh: lev: 16 (over y, x), wave: 64 (over z, core).
Axes of the slice: x: 4, y: 4, z: 32, core: 2. Of those that a mesh axis runs over, the one named last changes fastest.
Arguments:
- spectral: bfloat16 [128, 512, 3, 2, 512], P('lev', 'wave'), may hold values from -6 to 6
- modes_in: bfloat16 [128, 128], replicated, may hold values from -0.5 to 0.5
- modes_out: bfloat16 [128, 128], replicated, may hold values from -0.5 to 0.5
- mode_depth: float32 [128], replicated, may hold values from 0.1 to 10
- legendre: bfloat16 [512, 512, 256], P('wave'), may hold values from -0.25 to 0.25
- wave_map: int32 [512], replicated, may hold values from 0 to 511, as said below
- row_points: int32 [256], P('wave'), may hold values from 320 to 1280, as said below
Outputs:
- advected: float32 [3, 128, 256, 1280], P(None, 'lev', 'wave')
The draws below stay inside these ranges and needn't reach their ends.
Inputs may be any that keep to these rules, and one draw needn't show every extreme that they name: `wave_map`: a permutation of 0 to 511; the entries at slots 2 k and 2 k + 1 add up to 511. `row_points`: some row has all 1280 points.
All inputs are finite; a program needn't handle non-finite values.
Results may differ from the reference program's by a relative error of at most 0.0059.
Values may be sent and summed in bfloat16 or wider, within the bound.
No kernel may reach another device: no remote copies, remote signals or barrier semaphores. Data moves between devices by JAX's collectives and lax.ppermute only.
A program may use at most 32 MiB of HBM per device.

```python
import math
import jax
import jax.numpy as jnp
from jax import lax

LEVELS = 128
FIELDS = 3
LON = 1280
M_TOTAL = 512
LAT = 256


def draw_wave_map(key, part):
    shuffled = jax.random.permutation(jax.random.fold_in(key, 7), M_TOTAL // 2).astype(jnp.int32)
    lower_half = shuffled
    upper_half = M_TOTAL - 1 - shuffled
    return jnp.stack([lower_half, upper_half], axis=1).reshape(M_TOTAL).astype(jnp.int32)


def draw_row_points(key, part):
    first_key = jax.random.fold_in(key, 11)
    second_key = jax.random.fold_in(key, 12)
    row_counts = jax.random.randint(first_key, (LAT,), LON // 4, LON + 1, dtype=jnp.int32)
    widest = jax.random.randint(second_key, (), 0, LAT, dtype=jnp.int32)
    return jnp.where(jnp.arange(LAT, dtype=jnp.int32) == widest, LON, row_counts).astype(jnp.int32)


def levels(rng, dims, shards, least, high):
    level = 1.0
    for dim, parts in shards:
        draws = jax.random.uniform(jax.random.fold_in(jax.random.fold_in(rng, 6), dim), (parts,), jnp.float32, least / len(shards), high / len(shards))
        level = level * jnp.repeat(jnp.exp(draws), dims[dim] // parts).reshape((-1,) + (1,) * (len(dims) - 1 - dim))
    return level


def normal_values(stream_key, extent, deviation, reach, split=(), kind=jnp.bfloat16):
    array = deviation * jax.random.normal(stream_key, extent, jnp.float32)
    if split:
        array = array * levels(stream_key, extent, split, -0.22, 0.18)
    return jnp.clip(array, -reach, reach).astype(kind)


def setup_inputs(seed: int = 0) -> dict:
    streams_of = jax.random.split(jax.random.key(seed), 8)
    spectral = normal_values(streams_of[0], (LEVELS, M_TOTAL, FIELDS, 2, M_TOTAL), 1.0, 6.0, ((0, 16), (1, 64)))
    modes_in = normal_values(streams_of[1], (LEVELS, LEVELS), LEVELS ** -0.5, 0.5)
    modes_out = normal_values(streams_of[2], (LEVELS, LEVELS), LEVELS ** -0.5, 0.5)
    mode_depth = jnp.clip(jnp.exp(jax.random.uniform(streams_of[3], (LEVELS,), jnp.float32, math.log(0.1), math.log(10.0))), 0.1, 10.0)
    legendre = normal_values(streams_of[4], (M_TOTAL, M_TOTAL, LAT), M_TOTAL ** -0.5, 0.25, ((0, 64),))
    wave_map = draw_wave_map(jax.random.fold_in(streams_of[7], 71), 0)
    row_points = draw_row_points(jax.random.fold_in(streams_of[7], 71), 0)
    return dict(spectral=spectral, modes_in=modes_in, modes_out=modes_out, mode_depth=mode_depth, legendre=legendre, wave_map=wave_map, row_points=row_points)


time_step = 0.8

def damping(mode_depth, degree_of, degree_total):
    ratio = degree_of * (degree_of + 1.0) / float(degree_total * degree_total)
    return 1.0 / (1.0 + mode_depth[:, None] * ratio[None, :])

def trig_table(wave_map, lon_count):
    column = jnp.arange(lon_count, dtype=jnp.int32)
    product = wave_map[:, None] * column[None, :] % lon_count
    angles = product.astype(jnp.float32) * (2.0 * math.pi / lon_count)
    return jnp.stack([jnp.cos(angles), -jnp.sin(angles)], axis=1).astype(jnp.bfloat16)

def tendency(fields_ext):
    center = fields_ext[..., 1:-1, :]
    ahead_lon = jnp.roll(center, -1, axis=-1)
    behind_lon = jnp.roll(center, 1, axis=-1)
    ahead_lat = fields_ext[..., 2:, :]
    behind_lat = fields_ext[..., :-2, :]
    return center[0] * (ahead_lon - behind_lon) * 0.5 + center[1] * (ahead_lat - behind_lat) * 0.5

def pad_rows(values):
    return jnp.pad(values, ((0, 0), (1, 1), (0, 0)))

def reference(spectral, modes_in, modes_out, mode_depth, legendre, wave_map, row_points):
    degrees = jnp.arange(M_TOTAL, dtype=jnp.int32)
    keep_mask = degrees[None, :] >= wave_map[:, None]
    masked = jnp.where(keep_mask[None, :, None, None, :], spectral, jnp.zeros_like(spectral))
    flattened = masked.reshape(LEVELS, -1)
    modal_part = jnp.dot(modes_in, flattened, preferred_element_type=jnp.float32)
    degree_of = (jnp.arange(flattened.shape[1], dtype=jnp.int32) % M_TOTAL).astype(jnp.float32)
    scaled = (modal_part * damping(mode_depth, degree_of, M_TOTAL)).astype(jnp.bfloat16)
    solved = jnp.dot(modes_out, scaled, preferred_element_type=jnp.float32).astype(jnp.bfloat16)
    solved = solved.reshape(spectral.shape)
    trig_rows = trig_table(wave_map, LON).astype(jnp.float32)
    legendre_wide = legendre.astype(jnp.float32)
    points = jnp.arange(LON, dtype=jnp.int32)[None, :] < row_points[:, None]
    norm_factor = 1.0 / math.sqrt(M_TOTAL)

    def one_level(level_coef):
        band_rows = jnp.einsum('sfcn,snt->tsfc', level_coef.astype(jnp.float32), legendre_wide, precision=lax.Precision.HIGHEST).astype(jnp.bfloat16)
        grid_field = jnp.einsum('tsfc,scx->ftx', band_rows.astype(jnp.float32), trig_rows, precision=lax.Precision.HIGHEST) * norm_factor
        section_one = grid_field - time_step * tendency(pad_rows(grid_field))
        second = 0.5 * (grid_field + section_one - time_step * tendency(pad_rows(section_one)))
        return jnp.where(points[None, :, :], second, jnp.zeros_like(second))
    result = lax.map(one_level, solved)
    return jnp.transpose(result, (1, 0, 2, 3))
```

```python
import math

import jax
import jax.numpy as jnp
from jax import lax
from jax.sharding import PartitionSpec as P

LON = 1280


time_step = 0.8


def with_halo(value, sides, width):
    for axis, dim in sides:
        size, length = (lax.axis_size(axis), value.shape[dim])
        up = [(i, (i + 1) % size) for i in range(size - 1)]
        down = [(j, i) for i, j in up]
        last = lax.slice_in_dim(value, length - width, length, axis=dim)
        leading = lax.slice_in_dim(value, 0, width, axis=dim)
        before = lax.ppermute(last, axis, up)
        after = lax.ppermute(leading, axis, down)
        value = jnp.concatenate([before, value, after], axis=dim)
    return value


def damping(mode_depth, degree_of, degree_total):
    ratio = degree_of * (degree_of + 1.0) / float(degree_total * degree_total)
    return 1.0 / (1.0 + mode_depth[:, None] * ratio[None, :])


def trig_table(wave_map, lon_count, block=32):
    waves = wave_map[:, None]
    coarse = waves * (jnp.arange(lon_count // block, dtype=jnp.int32)[None, :] * block) % lon_count
    fine = waves * jnp.arange(block, dtype=jnp.int32)[None, :] % lon_count
    step = 2.0 * math.pi / lon_count
    coarse_angle = coarse.astype(jnp.float32) * step
    fine_angle = fine.astype(jnp.float32) * step
    cos_c, sin_c = jnp.cos(coarse_angle)[:, :, None], jnp.sin(coarse_angle)[:, :, None]
    cos_f, sin_f = jnp.cos(fine_angle)[:, None, :], jnp.sin(fine_angle)[:, None, :]
    cos_all = (cos_c * cos_f - sin_c * sin_f).reshape(wave_map.shape[0], lon_count)
    sin_all = (sin_c * cos_f + cos_c * sin_f).reshape(wave_map.shape[0], lon_count)
    return jnp.stack([cos_all, -sin_all], axis=1).astype(jnp.bfloat16)


def tendency(fields_ext):
    center = fields_ext[..., 1:-1, :]
    ahead_lon = jnp.roll(center, -1, axis=-1)
    behind_lon = jnp.roll(center, 1, axis=-1)
    ahead_lat = fields_ext[..., 2:, :]
    behind_lat = fields_ext[..., :-2, :]
    return center[0] * (ahead_lon - behind_lon) * 0.5 + center[1] * (ahead_lat - behind_lat) * 0.5


def column_solve(columns, modes_in, modes_out, mode_depth, degree_count):
    column_count = columns.shape[1]
    column_ids = lax.axis_index("lev") * column_count + jnp.arange(column_count, dtype=jnp.int32)
    degree_of = (column_ids % degree_count).astype(jnp.float32)
    modal_part = jnp.dot(modes_in, columns, preferred_element_type=jnp.float32)
    scaled = (modal_part * damping(mode_depth, degree_of, degree_count)).astype(jnp.bfloat16)
    return jnp.dot(modes_out, scaled, preferred_element_type=jnp.float32).astype(jnp.bfloat16)


def per_device(spectral, modes_in, modes_out, mode_depth, legendre, wave_map, row_points):
    lev_rows = spectral.shape[0]
    wave_slots = spectral.shape[1]
    field_count = spectral.shape[2]
    degree_count = spectral.shape[4]
    levels = modes_in.shape[0]
    shard_count = lax.axis_size("wave")
    first_slot = lax.axis_index("wave") * wave_slots
    local_waves = lax.dynamic_slice_in_dim(wave_map, first_slot, wave_slots)
    degrees = jnp.arange(degree_count, dtype=jnp.int32)
    keep_mask = degrees[None, :] >= local_waves[:, None]
    masked = jnp.where(keep_mask[None, :, None, None, :], spectral, jnp.zeros_like(spectral))
    flattened = masked.reshape(lev_rows, -1)
    trig_rows = trig_table(wave_map, LON).reshape(shard_count, wave_slots, 2, LON)
    norm_factor = 1.0 / math.sqrt(wave_map.shape[0])
    columns = lax.all_to_all(flattened, "lev", split_axis=1, concat_axis=0, tiled=True)
    solved_cols = column_solve(columns, modes_in, modes_out, mode_depth, degree_count)
    group_count = solved_cols.shape[1] // degree_count
    group_ids = lax.axis_index("lev") * group_count + jnp.arange(group_count, dtype=jnp.int32)
    slot_ids = group_ids // (field_count * 2)
    picked = jnp.take(legendre, slot_ids, axis=0)
    solved_groups = solved_cols.reshape(levels, group_count, degree_count)
    band_cols = jnp.einsum(
        "lgn,gnt->tgl", solved_groups, picked, preferred_element_type=jnp.float32
    ).astype(jnp.bfloat16)
    lev_count = lax.axis_size("lev")
    lat_rows = band_cols.shape[0] // shard_count
    outgoing = band_cols.reshape(shard_count, lat_rows, group_count, lev_count, lev_rows)
    outgoing = outgoing.transpose(3, 0, 1, 2, 4).reshape(lev_count * shard_count, -1)
    incoming = lax.all_to_all(outgoing, ("lev", "wave"), 0, 0, tiled=True)
    incoming = incoming.reshape(lev_count, shard_count, lat_rows, group_count, lev_rows)
    arrived = incoming.transpose(2, 1, 0, 3, 4).reshape(lat_rows, -1, lev_rows)
    split_bands = arrived.reshape(lat_rows, shard_count, wave_slots, field_count, 2, lev_rows)
    grid_field = (
        jnp.einsum("twsfcl,wscx->fltx", split_bands, trig_rows, preferred_element_type=jnp.float32)
        * norm_factor
    )
    wide_rows = with_halo(grid_field, (("wave", 2),), 2)
    section_wide = wide_rows[:, :, 1:-1, :] - time_step * tendency(wide_rows)
    second = 0.5 * (grid_field + section_wide[:, :, 1:-1, :] - time_step * tendency(section_wide))
    points = jnp.arange(LON, dtype=jnp.int32)[None, :] < row_points[:, None]
    return jnp.where(points[None, None, :, :], second, jnp.zeros_like(second))


def solution(mesh):
    in_specs = (
        P("lev", "wave", None, None, None),
        P(),
        P(),
        P(),
        P("wave", None, None),
        P(),
        P("wave"),
    )
    out_specs = P(None, "lev", "wave", None)
    return jax.shard_map(
        per_device, mesh=mesh, in_specs=in_specs, out_specs=out_specs, check_vma=False
    )
```

```python
import math

import jax
import jax.numpy as jnp
from jax import lax
from jax.sharding import PartitionSpec as P

LON = 1280


time_step = 0.8


def with_halo(value, sides, width):
    for axis, dim in sides:
        size, length = (lax.axis_size(axis), value.shape[dim])
        up = [(i, (i + 1) % size) for i in range(size - 1)]
        down = [(j, i) for i, j in up]
        last = lax.slice_in_dim(value, length - width, length, axis=dim)
        leading = lax.slice_in_dim(value, 0, width, axis=dim)
        before = lax.ppermute(last, axis, up)
        after = lax.ppermute(leading, axis, down)
        value = jnp.concatenate([before, value, after], axis=dim)
    return value


def wave_exchange(values, shard_count):
    chips = shard_count // 2
    rows = values.shape[0] // shard_count
    me = lax.axis_index("wave")
    chip, core = me // 2, me % 2
    parts = values.reshape(chips, 2, rows, *values.shape[1:])
    own = lax.dynamic_index_in_dim(parts, core, 1, keepdims=False)
    other = lax.dynamic_index_in_dim(parts, 1 - core, 1, keepdims=False)
    sibling = lax.ppermute(other, "wave", [(i, i ^ 1) for i in range(shard_count)])
    held = jnp.stack([own, sibling], axis=1)
    received = [lax.dynamic_index_in_dim(held, chip, 0, keepdims=False)]
    for shift in range(1, chips):
        send = lax.dynamic_index_in_dim(held, (chip + shift) % chips, 0, keepdims=False)
        pairs = [(i, ((i // 2 + shift) % chips) * 2 + i % 2) for i in range(shard_count)]
        received.append(lax.ppermute(send, "wave", pairs))
    by_shift = jnp.stack(received)
    by_chip = jnp.take(by_shift, (chip - jnp.arange(chips)) % chips, axis=0)
    by_core = jnp.where(core == 0, by_chip, jnp.flip(by_chip, axis=1))
    return jnp.swapaxes(by_core.reshape(shard_count, rows, *values.shape[1:]), 0, 1)


def damping(mode_depth, degree_of, degree_total):
    ratio = degree_of * (degree_of + 1.0) / float(degree_total * degree_total)
    return 1.0 / (1.0 + mode_depth[:, None] * ratio[None, :])


def trig_table(wave_map, lon_count, block=32):
    waves = wave_map[:, None]
    coarse = waves * (jnp.arange(lon_count // block, dtype=jnp.int32)[None, :] * block) % lon_count
    fine = waves * jnp.arange(block, dtype=jnp.int32)[None, :] % lon_count
    step = 2.0 * math.pi / lon_count
    coarse_angle = coarse.astype(jnp.float32) * step
    fine_angle = fine.astype(jnp.float32) * step
    cos_c, sin_c = jnp.cos(coarse_angle)[:, :, None], jnp.sin(coarse_angle)[:, :, None]
    cos_f, sin_f = jnp.cos(fine_angle)[:, None, :], jnp.sin(fine_angle)[:, None, :]
    cos_all = (cos_c * cos_f - sin_c * sin_f).reshape(wave_map.shape[0], lon_count)
    sin_all = (sin_c * cos_f + cos_c * sin_f).reshape(wave_map.shape[0], lon_count)
    return jnp.stack([cos_all, -sin_all], axis=1).astype(jnp.bfloat16)


def tendency(fields_ext):
    center = fields_ext[..., 1:-1, :]
    ahead_lon = jnp.roll(center, -1, axis=-1)
    behind_lon = jnp.roll(center, 1, axis=-1)
    ahead_lat = fields_ext[..., 2:, :]
    behind_lat = fields_ext[..., :-2, :]
    return center[0] * (ahead_lon - behind_lon) * 0.5 + center[1] * (ahead_lat - behind_lat) * 0.5


def column_solve(columns, modes_in, modes_out, mode_depth, degree_count):
    column_count = columns.shape[1]
    column_ids = lax.axis_index("lev") * column_count + jnp.arange(column_count, dtype=jnp.int32)
    degree_of = (column_ids % degree_count).astype(jnp.float32)
    modal_part = jnp.dot(modes_in, columns, preferred_element_type=jnp.float32)
    scaled = (modal_part * damping(mode_depth, degree_of, degree_count)).astype(jnp.bfloat16)
    return jnp.dot(modes_out, scaled, preferred_element_type=jnp.float32).astype(jnp.bfloat16)


def per_device(spectral, modes_in, modes_out, mode_depth, legendre, wave_map, row_points):
    lev_rows = spectral.shape[0]
    wave_slots = spectral.shape[1]
    field_count = spectral.shape[2]
    degree_count = spectral.shape[4]
    levels = modes_in.shape[0]
    shard_count = lax.axis_size("wave")
    first_slot = lax.axis_index("wave") * wave_slots
    local_waves = lax.dynamic_slice_in_dim(wave_map, first_slot, wave_slots)
    degrees = jnp.arange(degree_count, dtype=jnp.int32)
    keep_mask = degrees[None, :] >= local_waves[:, None]
    masked = jnp.where(keep_mask[None, :, None, None, :], spectral, jnp.zeros_like(spectral))
    flattened = masked.reshape(lev_rows, -1)
    trig_rows = trig_table(wave_map, LON).reshape(shard_count, wave_slots, 2, LON)
    norm_factor = 1.0 / math.sqrt(wave_map.shape[0])
    columns = lax.all_to_all(flattened, "lev", split_axis=1, concat_axis=0, tiled=True)
    solved_cols = column_solve(columns, modes_in, modes_out, mode_depth, degree_count)
    group_count = solved_cols.shape[1] // degree_count
    group_ids = lax.axis_index("lev") * group_count + jnp.arange(group_count, dtype=jnp.int32)
    slot_ids = group_ids // (field_count * 2)
    picked = jnp.take(legendre, slot_ids, axis=0)
    solved_groups = solved_cols.reshape(levels, group_count, degree_count)
    band_cols = jnp.einsum(
        "lgn,gnt->tgl", solved_groups, picked, preferred_element_type=jnp.float32
    ).astype(jnp.bfloat16)
    lev_sorted = lax.all_to_all(band_cols, "lev", split_axis=2, concat_axis=1, tiled=True)
    arrived = wave_exchange(lev_sorted, shard_count)
    lat_rows = arrived.shape[0]
    split_bands = arrived.reshape(lat_rows, shard_count, wave_slots, field_count, 2, lev_rows)
    grid_field = (
        jnp.einsum("twsfcl,wscx->fltx", split_bands, trig_rows, preferred_element_type=jnp.float32)
        * norm_factor
    )
    wide_rows = with_halo(grid_field, (("wave", 2),), 2)
    section_wide = wide_rows[:, :, 1:-1, :] - time_step * tendency(wide_rows)
    second = 0.5 * (grid_field + section_wide[:, :, 1:-1, :] - time_step * tendency(section_wide))
    points = jnp.arange(LON, dtype=jnp.int32)[None, :] < row_points[:, None]
    return jnp.where(points[None, None, :, :], second, jnp.zeros_like(second))


def solution(mesh):
    in_specs = (
        P("lev", "wave", None, None, None),
        P(),
        P(),
        P(),
        P("wave", None, None),
        P(),
        P("wave"),
    )
    out_specs = P(None, "lev", "wave", None)
    return jax.shard_map(
        per_device, mesh=mesh, in_specs=in_specs, out_specs=out_specs, check_vma=False
    )
```

```python
import math

import jax
import jax.numpy as jnp
from jax import lax
from jax.sharding import PartitionSpec as P

LON = 1280


time_step = 0.8


def with_halo(value, sides, width):
    for axis, dim in sides:
        size, length = (lax.axis_size(axis), value.shape[dim])
        up = [(i, (i + 1) % size) for i in range(size - 1)]
        down = [(j, i) for i, j in up]
        last = lax.slice_in_dim(value, length - width, length, axis=dim)
        leading = lax.slice_in_dim(value, 0, width, axis=dim)
        before = lax.ppermute(last, axis, up)
        after = lax.ppermute(leading, axis, down)
        value = jnp.concatenate([before, value, after], axis=dim)
    return value


def damping(mode_depth, degree_of, degree_total):
    ratio = degree_of * (degree_of + 1.0) / float(degree_total * degree_total)
    return 1.0 / (1.0 + mode_depth[:, None] * ratio[None, :])


def trig_table(wave_map, lon_count):
    column = jnp.arange(lon_count, dtype=jnp.int32)
    product = wave_map[:, None] * column[None, :] % lon_count
    angles = product.astype(jnp.float32) * (2.0 * math.pi / lon_count)
    return jnp.stack([jnp.cos(angles), -jnp.sin(angles)], axis=1).astype(jnp.bfloat16)


def tendency(fields_ext):
    center = fields_ext[..., 1:-1, :]
    ahead_lon = jnp.roll(center, -1, axis=-1)
    behind_lon = jnp.roll(center, 1, axis=-1)
    ahead_lat = fields_ext[..., 2:, :]
    behind_lat = fields_ext[..., :-2, :]
    return center[0] * (ahead_lon - behind_lon) * 0.5 + center[1] * (ahead_lat - behind_lat) * 0.5


def column_solve(columns, modes_in, modes_out, mode_depth, degree_count):
    column_count = columns.shape[1]
    column_ids = lax.axis_index("lev") * column_count + jnp.arange(column_count, dtype=jnp.int32)
    degree_of = (column_ids % degree_count).astype(jnp.float32)
    modal_part = jnp.dot(modes_in, columns, preferred_element_type=jnp.float32)
    scaled = (modal_part * damping(mode_depth, degree_of, degree_count)).astype(jnp.bfloat16)
    return jnp.dot(modes_out, scaled, preferred_element_type=jnp.float32).astype(jnp.bfloat16)


def per_device(spectral, modes_in, modes_out, mode_depth, legendre, wave_map, row_points):
    lev_rows = spectral.shape[0]
    wave_slots = spectral.shape[1]
    field_count = spectral.shape[2]
    degree_count = spectral.shape[4]
    levels = modes_in.shape[0]
    shard_count = lax.axis_size("wave")
    first_slot = lax.axis_index("wave") * wave_slots
    local_waves = lax.dynamic_slice_in_dim(wave_map, first_slot, wave_slots)
    flattened = spectral.reshape(lev_rows, -1)
    trig_rows = trig_table(wave_map, LON).reshape(shard_count, wave_slots, 2, LON)
    norm_factor = 1.0 / math.sqrt(wave_map.shape[0])
    columns = lax.all_to_all(flattened, "lev", split_axis=1, concat_axis=0, tiled=True)
    column_count = columns.shape[1]
    column_ids = lax.axis_index("lev") * column_count + jnp.arange(column_count, dtype=jnp.int32)
    column_waves = jnp.take(local_waves, column_ids // (degree_count * field_count * 2))
    keep_mask = column_ids % degree_count >= column_waves
    columns = jnp.where(keep_mask[None, :], columns, jnp.zeros_like(columns))
    solved_cols = column_solve(columns, modes_in, modes_out, mode_depth, degree_count)
    group_count = solved_cols.shape[1] // degree_count
    group_ids = lax.axis_index("lev") * group_count + jnp.arange(group_count, dtype=jnp.int32)
    slot_ids = group_ids // (field_count * 2)
    picked = jnp.take(legendre, slot_ids, axis=0)
    solved_groups = solved_cols.reshape(levels, group_count, degree_count)
    band_cols = jnp.einsum(
        "lgn,gnt->tgl", solved_groups, picked, preferred_element_type=jnp.float32
    ).astype(jnp.bfloat16)
    arrived = lax.all_to_all(
        lax.all_to_all(band_cols, "lev", split_axis=2, concat_axis=1, tiled=True),
        "wave",
        split_axis=0,
        concat_axis=2,
        tiled=True,
    )
    lat_rows = arrived.shape[0]

    def synthesis(bands):
        split_bands = bands.reshape(bands.shape[0], wave_slots, field_count, 2, shard_count, lev_rows)
        return (
            jnp.einsum("tsfcwl,wscx->fltx", split_bands, trig_rows, preferred_element_type=jnp.float32)
            * norm_factor
        )

    band_halo = with_halo(arrived, (("wave", 0),), 2)
    grid_field = synthesis(arrived)
    halo_grid = synthesis(jnp.concatenate([band_halo[:2], band_halo[-2:]], axis=0))
    wide_rows = jnp.concatenate([halo_grid[:, :, :2], grid_field, halo_grid[:, :, 2:]], axis=2)
    section_wide = wide_rows[:, :, 1:-1, :] - time_step * tendency(wide_rows)
    second = 0.5 * (grid_field + section_wide[:, :, 1:-1, :] - time_step * tendency(section_wide))
    points = jnp.arange(LON, dtype=jnp.int32)[None, :] < row_points[:, None]
    return jnp.where(points[None, None, :, :], second, jnp.zeros_like(second))


def solution(mesh):
    in_specs = (
        P("lev", "wave", None, None, None),
        P(),
        P(),
        P(),
        P("wave", None, None),
        P(),
        P("wave"),
    )
    out_specs = P(None, "lev", "wave", None)
    return jax.shard_map(
        per_device, mesh=mesh, in_specs=in_specs, out_specs=out_specs, check_vma=False
    )
```

```python
import math

import jax
import jax.numpy as jnp
from jax import lax
from jax.sharding import PartitionSpec as P

LON = 1280


time_step = 0.8


def with_halo(value, sides, width):
    for axis, dim in sides:
        size, length = (lax.axis_size(axis), value.shape[dim])
        up = [(i, (i + 1) % size) for i in range(size - 1)]
        down = [(j, i) for i, j in up]
        last = lax.slice_in_dim(value, length - width, length, axis=dim)
        leading = lax.slice_in_dim(value, 0, width, axis=dim)
        before = lax.ppermute(last, axis, up)
        after = lax.ppermute(leading, axis, down)
        value = jnp.concatenate([before, value, after], axis=dim)
    return value


def damping(mode_depth, degree_of, degree_total):
    ratio = degree_of * (degree_of + 1.0) / float(degree_total * degree_total)
    return 1.0 / (1.0 + mode_depth[:, None] * ratio[None, :])


def trig_table(wave_map, lon_count):
    column = jnp.arange(lon_count, dtype=jnp.int32)
    product = wave_map[:, None] * column[None, :] % lon_count
    angles = product.astype(jnp.float32) * (2.0 * math.pi / lon_count)
    return jnp.stack([jnp.cos(angles), -jnp.sin(angles)], axis=1).astype(jnp.bfloat16)


def tendency(fields_ext):
    center = fields_ext[..., 1:-1, :]
    ahead_lon = jnp.roll(center, -1, axis=-1)
    behind_lon = jnp.roll(center, 1, axis=-1)
    ahead_lat = fields_ext[..., 2:, :]
    behind_lat = fields_ext[..., :-2, :]
    return center[0] * (ahead_lon - behind_lon) * 0.5 + center[1] * (ahead_lat - behind_lat) * 0.5


def column_solve(columns, modes_in, modes_out, mode_depth, degree_count):
    column_count = columns.shape[1]
    column_ids = lax.axis_index("lev") * column_count + jnp.arange(column_count, dtype=jnp.int32)
    degree_of = (column_ids % degree_count).astype(jnp.float32)
    modal_part = jnp.dot(modes_in, columns, preferred_element_type=jnp.float32)
    scaled = (modal_part * damping(mode_depth, degree_of, degree_count)).astype(jnp.bfloat16)
    return jnp.dot(modes_out, scaled, preferred_element_type=jnp.float32).astype(jnp.bfloat16)


def per_device(spectral, modes_in, modes_out, mode_depth, legendre, wave_map, row_points):
    lev_rows = spectral.shape[0]
    wave_slots = spectral.shape[1]
    field_count = spectral.shape[2]
    degree_count = spectral.shape[4]
    levels = modes_in.shape[0]
    shard_count = lax.axis_size("wave")
    first_slot = lax.axis_index("wave") * wave_slots
    local_waves = lax.dynamic_slice_in_dim(wave_map, first_slot, wave_slots)
    flattened = spectral.reshape(lev_rows, -1)
    trig_rows = trig_table(wave_map, LON).reshape(shard_count, wave_slots, 2, LON)
    norm_factor = 1.0 / math.sqrt(wave_map.shape[0])
    columns = lax.all_to_all(flattened, "lev", split_axis=1, concat_axis=0, tiled=True)
    column_count = columns.shape[1]
    column_ids = lax.axis_index("lev") * column_count + jnp.arange(column_count, dtype=jnp.int32)
    column_waves = jnp.take(local_waves, column_ids // (degree_count * field_count * 2))
    keep_mask = column_ids % degree_count >= column_waves
    columns = jnp.where(keep_mask[None, :], columns, jnp.zeros_like(columns))
    solved_cols = column_solve(columns, modes_in, modes_out, mode_depth, degree_count)
    group_count = solved_cols.shape[1] // degree_count
    group_ids = lax.axis_index("lev") * group_count + jnp.arange(group_count, dtype=jnp.int32)
    slot_ids = group_ids // (field_count * 2)
    picked = jnp.take(legendre, slot_ids, axis=0)
    solved_groups = solved_cols.reshape(levels, group_count, degree_count)
    band_cols = jnp.einsum(
        "lgn,gnt->tgl", solved_groups, picked, preferred_element_type=jnp.float32
    ).astype(jnp.bfloat16)
    arrived = lax.all_to_all(
        lax.all_to_all(band_cols, "lev", split_axis=2, concat_axis=1, tiled=True),
        "wave",
        split_axis=0,
        concat_axis=2,
        tiled=True,
    )
    lat_rows = arrived.shape[0]

    split_bands = arrived.reshape(lat_rows, wave_slots, field_count, 2, shard_count, lev_rows)

    def synthesis(bands):
        return (
            jnp.einsum("tsfcwl,wscx->fltx", bands, trig_rows, preferred_element_type=jnp.float32)
            * norm_factor
        )

    up = [(i, i + 1) for i in range(shard_count - 1)]
    down = [(j, i) for i, j in up]
    before = lax.ppermute(split_bands[lat_rows - 2:], "wave", up)
    after = lax.ppermute(split_bands[:2], "wave", down)
    grid_field = synthesis(split_bands)
    halo_grid = synthesis(jnp.concatenate([before, after], axis=0))
    wide_rows = jnp.concatenate([halo_grid[:, :, :2], grid_field, halo_grid[:, :, 2:]], axis=2)
    section_wide = wide_rows[:, :, 1:-1, :] - time_step * tendency(wide_rows)
    second = 0.5 * (grid_field + section_wide[:, :, 1:-1, :] - time_step * tendency(section_wide))
    points = jnp.arange(LON, dtype=jnp.int32)[None, :] < row_points[:, None]
    return jnp.where(points[None, None, :, :], second, jnp.zeros_like(second))


def solution(mesh):
    in_specs = (
        P("lev", "wave", None, None, None),
        P(),
        P(),
        P(),
        P("wave", None, None),
        P(),
        P("wave"),
    )
    out_specs = P(None, "lev", "wave", None)
    return jax.shard_map(
        per_device, mesh=mesh, in_specs=in_specs, out_specs=out_specs, check_vma=False
    )
```

```python
import math

import jax
import jax.numpy as jnp
from jax import lax
from jax.sharding import Mesh, PartitionSpec as P

LON = 1280


time_step = 0.8


def with_halo(value, sides, width):
    for axis, dim in sides:
        size, length = (lax.axis_size(axis), value.shape[dim])
        up = [(i, (i + 1) % size) for i in range(size - 1)]
        down = [(j, i) for i, j in up]
        last = lax.slice_in_dim(value, length - width, length, axis=dim)
        leading = lax.slice_in_dim(value, 0, width, axis=dim)
        before = lax.ppermute(last, axis, up)
        after = lax.ppermute(leading, axis, down)
        value = jnp.concatenate([before, value, after], axis=dim)
    return value


def lev_exchange(value, split_axis, concat_axis):
    rows, cols = lax.axis_size("lev_y"), lax.axis_size("lev_x")
    shape = value.shape
    parts = value.reshape(*shape[:split_axis], rows, cols, shape[split_axis] // (rows * cols), *shape[split_axis + 1:])
    parts = lax.all_to_all(parts, "lev_x", split_axis=split_axis + 1, concat_axis=concat_axis, tiled=True)
    parts = lax.all_to_all(parts, "lev_y", split_axis=split_axis, concat_axis=concat_axis, tiled=True)
    out_shape = list(shape)
    out_shape[split_axis] //= rows * cols
    out_shape[concat_axis] *= rows * cols
    return parts.reshape(out_shape)


def damping(mode_depth, degree_of, degree_total):
    ratio = degree_of * (degree_of + 1.0) / float(degree_total * degree_total)
    return 1.0 / (1.0 + mode_depth[:, None] * ratio[None, :])


def trig_table(wave_map, lon_count):
    column = jnp.arange(lon_count, dtype=jnp.int32)
    product = wave_map[:, None] * column[None, :] % lon_count
    angles = product.astype(jnp.float32) * (2.0 * math.pi / lon_count)
    return jnp.stack([jnp.cos(angles), -jnp.sin(angles)], axis=1).astype(jnp.bfloat16)


def tendency(fields_ext):
    center = fields_ext[..., 1:-1, :]
    ahead_lon = jnp.roll(center, -1, axis=-1)
    behind_lon = jnp.roll(center, 1, axis=-1)
    ahead_lat = fields_ext[..., 2:, :]
    behind_lat = fields_ext[..., :-2, :]
    return center[0] * (ahead_lon - behind_lon) * 0.5 + center[1] * (ahead_lat - behind_lat) * 0.5


def column_solve(columns, modes_in, modes_out, mode_depth, degree_count):
    column_count = columns.shape[1]
    column_ids = lax.axis_index(("lev_y", "lev_x")) * column_count + jnp.arange(column_count, dtype=jnp.int32)
    degree_of = (column_ids % degree_count).astype(jnp.float32)
    modal_part = jnp.dot(modes_in, columns, preferred_element_type=jnp.float32)
    scaled = (modal_part * damping(mode_depth, degree_of, degree_count)).astype(jnp.bfloat16)
    return jnp.dot(modes_out, scaled, preferred_element_type=jnp.float32).astype(jnp.bfloat16)


def per_device(spectral, modes_in, modes_out, mode_depth, legendre, wave_map, row_points):
    lev_rows = spectral.shape[0]
    wave_slots = spectral.shape[1]
    field_count = spectral.shape[2]
    degree_count = spectral.shape[4]
    levels = modes_in.shape[0]
    shard_count = lax.axis_size("wave")
    first_slot = lax.axis_index("wave") * wave_slots
    local_waves = lax.dynamic_slice_in_dim(wave_map, first_slot, wave_slots)
    flattened = spectral.reshape(lev_rows, -1)
    trig_rows = trig_table(wave_map, LON).reshape(shard_count, wave_slots, 2, LON)
    norm_factor = 1.0 / math.sqrt(wave_map.shape[0])
    columns = lev_exchange(flattened, 1, 0)
    column_count = columns.shape[1]
    column_ids = lax.axis_index(("lev_y", "lev_x")) * column_count + jnp.arange(column_count, dtype=jnp.int32)
    column_waves = jnp.take(local_waves, column_ids // (degree_count * field_count * 2))
    keep_mask = column_ids % degree_count >= column_waves
    columns = jnp.where(keep_mask[None, :], columns, jnp.zeros_like(columns))
    solved_cols = column_solve(columns, modes_in, modes_out, mode_depth, degree_count)
    group_count = solved_cols.shape[1] // degree_count
    group_ids = lax.axis_index(("lev_y", "lev_x")) * group_count + jnp.arange(group_count, dtype=jnp.int32)
    slot_ids = group_ids // (field_count * 2)
    picked = jnp.take(legendre, slot_ids, axis=0)
    solved_groups = solved_cols.reshape(levels, group_count, degree_count)
    band_cols = jnp.einsum(
        "lgn,gnt->tgl", solved_groups, picked, preferred_element_type=jnp.float32
    ).astype(jnp.bfloat16)
    arrived = lax.all_to_all(
        lev_exchange(band_cols, 2, 1),
        "wave",
        split_axis=0,
        concat_axis=2,
        tiled=True,
    )
    lat_rows = arrived.shape[0]

    split_bands = arrived.reshape(lat_rows, wave_slots, field_count, 2, shard_count, lev_rows)

    def synthesis(bands):
        return (
            jnp.einsum("tsfcwl,wscx->fltx", bands, trig_rows, preferred_element_type=jnp.float32)
            * norm_factor
        )

    up = [(i, i + 1) for i in range(shard_count - 1)]
    down = [(j, i) for i, j in up]
    before = lax.ppermute(split_bands[lat_rows - 2:], "wave", up)
    after = lax.ppermute(split_bands[:2], "wave", down)
    grid_field = synthesis(split_bands)
    halo_grid = synthesis(jnp.concatenate([before, after], axis=0))
    wide_rows = jnp.concatenate([halo_grid[:, :, :2], grid_field, halo_grid[:, :, 2:]], axis=2)
    section_wide = wide_rows[:, :, 1:-1, :] - time_step * tendency(wide_rows)
    second = 0.5 * (grid_field + section_wide[:, :, 1:-1, :] - time_step * tendency(section_wide))
    points = jnp.arange(LON, dtype=jnp.int32)[None, :] < row_points[:, None]
    return jnp.where(points[None, None, :, :], second, jnp.zeros_like(second))


def solution(mesh):
    lev_y = 4 if mesh.shape["lev"] % 4 == 0 else 1
    split = Mesh(
        mesh.devices.reshape(lev_y, mesh.shape["lev"] // lev_y, mesh.shape["wave"]),
        ("lev_y", "lev_x", "wave"),
    )
    lev = ("lev_y", "lev_x")
    in_specs = (
        P(lev, "wave", None, None, None),
        P(),
        P(),
        P(),
        P("wave", None, None),
        P(),
        P("wave"),
    )
    out_specs = P(None, lev, "wave", None)
    return jax.shard_map(
        per_device, mesh=split, in_specs=in_specs, out_specs=out_specs, check_vma=False
    )
```

```python
import math

import jax
import jax.numpy as jnp
from jax import lax
from jax.sharding import PartitionSpec as P

LON = 1280


time_step = 0.8


def with_halo(value, sides, width):
    for axis, dim in sides:
        size, length = (lax.axis_size(axis), value.shape[dim])
        up = [(i, (i + 1) % size) for i in range(size - 1)]
        down = [(j, i) for i, j in up]
        last = lax.slice_in_dim(value, length - width, length, axis=dim)
        leading = lax.slice_in_dim(value, 0, width, axis=dim)
        before = lax.ppermute(last, axis, up)
        after = lax.ppermute(leading, axis, down)
        value = jnp.concatenate([before, value, after], axis=dim)
    return value


def damping(mode_depth, degree_of, degree_total):
    ratio = degree_of * (degree_of + 1.0) / float(degree_total * degree_total)
    return 1.0 / (1.0 + mode_depth[:, None] * ratio[None, :])


def trig_table(wave_map, lon_count):
    column = jnp.arange(lon_count, dtype=jnp.int32)
    product = wave_map[:, None] * column[None, :] % lon_count
    angles = product.astype(jnp.float32) * (2.0 * math.pi / lon_count)
    return jnp.stack([jnp.cos(angles), -jnp.sin(angles)], axis=1).astype(jnp.bfloat16)


def tendency(fields_ext):
    center = fields_ext[..., 1:-1, :]
    ahead_lon = jnp.roll(center, -1, axis=-1)
    behind_lon = jnp.roll(center, 1, axis=-1)
    ahead_lat = fields_ext[..., 2:, :]
    behind_lat = fields_ext[..., :-2, :]
    return center[0] * (ahead_lon - behind_lon) * 0.5 + center[1] * (ahead_lat - behind_lat) * 0.5


def column_solve(columns, modes_in, modes_out, mode_depth, degree_count):
    column_count = columns.shape[1]
    column_ids = lax.axis_index("lev") * column_count + jnp.arange(column_count, dtype=jnp.int32)
    degree_of = (column_ids % degree_count).astype(jnp.float32)
    modal_part = jnp.dot(modes_in, columns, preferred_element_type=jnp.float32)
    scaled = (modal_part * damping(mode_depth, degree_of, degree_count)).astype(jnp.bfloat16)
    return jnp.dot(modes_out, scaled, preferred_element_type=jnp.float32).astype(jnp.bfloat16)


def per_device(spectral, modes_in, modes_out, mode_depth, legendre, wave_map, row_points):
    lev_rows = spectral.shape[0]
    wave_slots = spectral.shape[1]
    field_count = spectral.shape[2]
    degree_count = spectral.shape[4]
    levels = modes_in.shape[0]
    shard_count = lax.axis_size("wave")
    first_slot = lax.axis_index("wave") * wave_slots
    local_waves = lax.dynamic_slice_in_dim(wave_map, first_slot, wave_slots)
    flattened = spectral.reshape(lev_rows, -1)
    trig_rows = trig_table(wave_map, LON).reshape(shard_count, wave_slots, 2, LON)
    norm_factor = 1.0 / math.sqrt(wave_map.shape[0])
    columns = lax.all_to_all(flattened, "lev", split_axis=1, concat_axis=0, tiled=True)
    column_count = columns.shape[1]
    column_ids = lax.axis_index("lev") * column_count + jnp.arange(column_count, dtype=jnp.int32)
    column_waves = jnp.take(local_waves, column_ids // (degree_count * field_count * 2))
    keep_mask = column_ids % degree_count >= column_waves
    columns = jnp.where(keep_mask[None, :], columns, jnp.zeros_like(columns))
    solved_cols = column_solve(columns, modes_in, modes_out, mode_depth, degree_count)
    group_count = solved_cols.shape[1] // degree_count
    group_ids = lax.axis_index("lev") * group_count + jnp.arange(group_count, dtype=jnp.int32)
    slot_ids = group_ids // (field_count * 2)
    picked = jnp.take(legendre, slot_ids, axis=0)
    solved_groups = solved_cols.reshape(levels, group_count, degree_count)
    band_cols = jnp.einsum(
        "lgn,gnt->tgl", solved_groups, picked, preferred_element_type=jnp.float32
    ).astype(jnp.bfloat16)
    arrived = lax.all_to_all(
        lax.all_to_all(band_cols, "lev", split_axis=2, concat_axis=1, tiled=True),
        "wave",
        split_axis=0,
        concat_axis=2,
        tiled=True,
    )
    lat_rows = arrived.shape[0]

    split_bands = arrived.reshape(lat_rows, wave_slots, field_count, 2, shard_count, lev_rows)

    def synthesis(bands):
        ordered = bands.transpose(2, 5, 0, 1, 3, 4)
        return (
            jnp.einsum("fltscw,wscx->fltx", ordered, trig_rows, preferred_element_type=jnp.float32)
            * norm_factor
        )

    up = [(i, i + 1) for i in range(shard_count - 1)]
    down = [(j, i) for i, j in up]
    before = lax.ppermute(split_bands[lat_rows - 2:], "wave", up)
    after = lax.ppermute(split_bands[:2], "wave", down)
    grid_field = synthesis(split_bands)
    halo_grid = synthesis(jnp.concatenate([before, after], axis=0))
    wide_rows = jnp.concatenate([halo_grid[:, :, :2], grid_field, halo_grid[:, :, 2:]], axis=2)
    section_wide = wide_rows[:, :, 1:-1, :] - time_step * tendency(wide_rows)
    second = 0.5 * (grid_field + section_wide[:, :, 1:-1, :] - time_step * tendency(section_wide))
    points = jnp.arange(LON, dtype=jnp.int32)[None, :] < row_points[:, None]
    return jnp.where(points[None, None, :, :], second, jnp.zeros_like(second))


def solution(mesh):
    in_specs = (
        P("lev", "wave", None, None, None),
        P(),
        P(),
        P(),
        P("wave", None, None),
        P(),
        P("wave"),
    )
    out_specs = P(None, "lev", "wave", None)
    return jax.shard_map(
        per_device, mesh=mesh, in_specs=in_specs, out_specs=out_specs, check_vma=False
    )
```

```python
import math

import jax
import jax.numpy as jnp
from jax import lax
from jax.sharding import PartitionSpec as P

LON = 1280


time_step = 0.8


def with_halo(value, sides, width):
    for axis, dim in sides:
        size, length = (lax.axis_size(axis), value.shape[dim])
        up = [(i, (i + 1) % size) for i in range(size - 1)]
        down = [(j, i) for i, j in up]
        last = lax.slice_in_dim(value, length - width, length, axis=dim)
        leading = lax.slice_in_dim(value, 0, width, axis=dim)
        before = lax.ppermute(last, axis, up)
        after = lax.ppermute(leading, axis, down)
        value = jnp.concatenate([before, value, after], axis=dim)
    return value


def damping(mode_depth, degree_of, degree_total):
    ratio = degree_of * (degree_of + 1.0) / float(degree_total * degree_total)
    return 1.0 / (1.0 + mode_depth[:, None] * ratio[None, :])


def trig_table(wave_map, lon_count):
    column = jnp.arange(lon_count, dtype=jnp.int32)
    product = wave_map[:, None] * column[None, :] % lon_count
    angles = product.astype(jnp.float32) * (2.0 * math.pi / lon_count)
    return jnp.stack([jnp.cos(angles), -jnp.sin(angles)], axis=1).astype(jnp.bfloat16)


def tendency(fields_ext):
    center = fields_ext[..., 1:-1, :]
    ahead_lon = jnp.roll(center, -1, axis=-1)
    behind_lon = jnp.roll(center, 1, axis=-1)
    ahead_lat = fields_ext[..., 2:, :]
    behind_lat = fields_ext[..., :-2, :]
    return center[0] * (ahead_lon - behind_lon) * 0.5 + center[1] * (ahead_lat - behind_lat) * 0.5


def column_solve(columns, modes_in, modes_out, mode_depth, degree_count):
    column_count = columns.shape[1]
    column_ids = lax.axis_index("lev") * column_count + jnp.arange(column_count, dtype=jnp.int32)
    degree_of = (column_ids % degree_count).astype(jnp.float32)
    modal_part = jnp.dot(modes_in, columns, preferred_element_type=jnp.float32)
    scaled = (modal_part * damping(mode_depth, degree_of, degree_count)).astype(jnp.bfloat16)
    return jnp.dot(modes_out, scaled, preferred_element_type=jnp.float32).astype(jnp.bfloat16)


def per_device(spectral, modes_in, modes_out, mode_depth, legendre, wave_map, row_points):
    lev_rows = spectral.shape[0]
    wave_slots = spectral.shape[1]
    field_count = spectral.shape[2]
    degree_count = spectral.shape[4]
    levels = modes_in.shape[0]
    shard_count = lax.axis_size("wave")
    first_slot = lax.axis_index("wave") * wave_slots
    local_waves = lax.dynamic_slice_in_dim(wave_map, first_slot, wave_slots)
    flattened = spectral.reshape(lev_rows, -1)
    trig_rows = trig_table(wave_map, LON).reshape(shard_count, wave_slots, 2, LON)
    norm_factor = 1.0 / math.sqrt(wave_map.shape[0])
    columns = lax.all_to_all(flattened, "lev", split_axis=1, concat_axis=0, tiled=True)
    column_count = columns.shape[1]
    column_ids = lax.axis_index("lev") * column_count + jnp.arange(column_count, dtype=jnp.int32)
    column_waves = jnp.take(local_waves, column_ids // (degree_count * field_count * 2))
    keep_mask = column_ids % degree_count >= column_waves
    columns = jnp.where(keep_mask[None, :], columns, jnp.zeros_like(columns))
    solved_cols = column_solve(columns, modes_in, modes_out, mode_depth, degree_count)
    group_count = solved_cols.shape[1] // degree_count
    group_ids = lax.axis_index("lev") * group_count + jnp.arange(group_count, dtype=jnp.int32)
    slot_ids = group_ids // (field_count * 2)
    picked = jnp.take(legendre, slot_ids, axis=0)
    solved_groups = solved_cols.reshape(levels, group_count, degree_count)
    band_cols = jnp.einsum(
        "lgn,gnt->tgl", solved_groups, picked, preferred_element_type=jnp.float32
    ).astype(jnp.bfloat16)
    arrived = lax.all_to_all(
        lax.all_to_all(band_cols, "lev", split_axis=2, concat_axis=1, tiled=True),
        "wave",
        split_axis=0,
        concat_axis=2,
        tiled=True,
    )
    lat_rows = arrived.shape[0]
    split_bands = arrived.reshape(lat_rows, wave_slots, field_count, 2, shard_count, lev_rows)
    grid_field = (
        jnp.einsum("tsfcwl,wscx->fltx", split_bands, trig_rows, preferred_element_type=jnp.float32)
        * norm_factor
    )
    wide_rows = with_halo(grid_field, (("wave", 2),), 2)
    section_wide = wide_rows[:, :, 1:-1, :] - time_step * tendency(wide_rows)
    second = 0.5 * (grid_field + section_wide[:, :, 1:-1, :] - time_step * tendency(section_wide))
    points = jnp.arange(LON, dtype=jnp.int32)[None, :] < row_points[:, None]
    return jnp.where(points[None, None, :, :], second, jnp.zeros_like(second))


def solution(mesh):
    in_specs = (
        P("lev", "wave", None, None, None),
        P(),
        P(),
        P(),
        P("wave", None, None),
        P(),
        P("wave"),
    )
    out_specs = P(None, "lev", "wave", None)
    return jax.shard_map(
        per_device, mesh=mesh, in_specs=in_specs, out_specs=out_specs, check_vma=False
    )
```

```python
import math

import jax
import jax.numpy as jnp
from jax import lax
from jax.sharding import PartitionSpec as P

LON = 1280


time_step = 0.8


def with_halo(value, sides, width):
    for axis, dim in sides:
        size, length = (lax.axis_size(axis), value.shape[dim])
        up = [(i, (i + 1) % size) for i in range(size - 1)]
        down = [(j, i) for i, j in up]
        last = lax.slice_in_dim(value, length - width, length, axis=dim)
        leading = lax.slice_in_dim(value, 0, width, axis=dim)
        before = lax.ppermute(last, axis, up)
        after = lax.ppermute(leading, axis, down)
        value = jnp.concatenate([before, value, after], axis=dim)
    return value


def damping(mode_depth, degree_of, degree_total):
    ratio = degree_of * (degree_of + 1.0) / float(degree_total * degree_total)
    return 1.0 / (1.0 + mode_depth[:, None] * ratio[None, :])


def trig_table(wave_map, lon_count):
    column = jnp.arange(lon_count, dtype=jnp.int32)
    product = wave_map[:, None] * column[None, :] % lon_count
    angles = product.astype(jnp.float32) * (2.0 * math.pi / lon_count)
    return jnp.stack([jnp.cos(angles), -jnp.sin(angles)], axis=1).astype(jnp.bfloat16)


def tendency(fields_ext):
    center = fields_ext[..., 1:-1, :]
    ahead_lon = jnp.roll(center, -1, axis=-1)
    behind_lon = jnp.roll(center, 1, axis=-1)
    ahead_lat = fields_ext[..., 2:, :]
    behind_lat = fields_ext[..., :-2, :]
    return center[0] * (ahead_lon - behind_lon) * 0.5 + center[1] * (ahead_lat - behind_lat) * 0.5


def column_solve(columns, modes_in, modes_out, mode_depth, degree_count):
    column_count = columns.shape[1]
    column_ids = lax.axis_index("lev") * column_count + jnp.arange(column_count, dtype=jnp.int32)
    degree_of = (column_ids % degree_count).astype(jnp.float32)
    modal_part = jnp.dot(modes_in, columns, preferred_element_type=jnp.float32)
    scaled = (modal_part * damping(mode_depth, degree_of, degree_count)).astype(jnp.bfloat16)
    return jnp.dot(modes_out, scaled, preferred_element_type=jnp.float32).astype(jnp.bfloat16)


def per_device(spectral, modes_in, modes_out, mode_depth, legendre, wave_map, row_points):
    lev_rows = spectral.shape[0]
    wave_slots = spectral.shape[1]
    field_count = spectral.shape[2]
    degree_count = spectral.shape[4]
    levels = modes_in.shape[0]
    shard_count = lax.axis_size("wave")
    first_slot = lax.axis_index("wave") * wave_slots
    local_waves = lax.dynamic_slice_in_dim(wave_map, first_slot, wave_slots)
    degrees = jnp.arange(degree_count, dtype=jnp.int32)
    keep_mask = degrees[None, :] >= local_waves[:, None]
    masked = jnp.where(keep_mask[None, :, None, None, :], spectral, jnp.zeros_like(spectral))
    flattened = masked.reshape(lev_rows, -1)
    trig_rows = trig_table(wave_map, LON).reshape(shard_count, wave_slots, 2, LON)
    norm_factor = 1.0 / math.sqrt(wave_map.shape[0])
    columns = lax.all_to_all(flattened, "lev", split_axis=1, concat_axis=0, tiled=True)
    solved_cols = column_solve(columns, modes_in, modes_out, mode_depth, degree_count)
    group_count = solved_cols.shape[1] // degree_count
    group_ids = lax.axis_index("lev") * group_count + jnp.arange(group_count, dtype=jnp.int32)
    slot_ids = group_ids // (field_count * 2)
    picked = jnp.take(legendre, slot_ids, axis=0)
    solved_groups = solved_cols.reshape(levels, group_count, degree_count)
    band_cols = jnp.einsum(
        "lgn,gnt->tgl", solved_groups, picked, preferred_element_type=jnp.float32
    ).astype(jnp.bfloat16)
    arrived = lax.all_to_all(
        lax.all_to_all(band_cols, "lev", split_axis=2, concat_axis=1, tiled=True),
        "wave",
        split_axis=0,
        concat_axis=2,
        tiled=True,
    )
    lat_rows = arrived.shape[0]

    split_bands = arrived.reshape(lat_rows, wave_slots, field_count, 2, shard_count, lev_rows)

    def synthesis(bands):
        return (
            jnp.einsum("tsfcwl,wscx->fltx", bands, trig_rows, preferred_element_type=jnp.float32)
            * norm_factor
        )

    up = [(i, i + 1) for i in range(shard_count - 1)]
    down = [(j, i) for i, j in up]
    before = lax.ppermute(split_bands[lat_rows - 2:], "wave", up)
    after = lax.ppermute(split_bands[:2], "wave", down)
    grid_field = synthesis(split_bands)
    halo_grid = synthesis(jnp.concatenate([before, after], axis=0))
    wide_rows = jnp.concatenate([halo_grid[:, :, :2], grid_field, halo_grid[:, :, 2:]], axis=2)
    section_wide = wide_rows[:, :, 1:-1, :] - time_step * tendency(wide_rows)
    second = 0.5 * (grid_field + section_wide[:, :, 1:-1, :] - time_step * tendency(section_wide))
    points = jnp.arange(LON, dtype=jnp.int32)[None, :] < row_points[:, None]
    return jnp.where(points[None, None, :, :], second, jnp.zeros_like(second))


def solution(mesh):
    in_specs = (
        P("lev", "wave", None, None, None),
        P(),
        P(),
        P(),
        P("wave", None, None),
        P(),
        P("wave"),
    )
    out_specs = P(None, "lev", "wave", None)
    return jax.shard_map(
        per_device, mesh=mesh, in_specs=in_specs, out_specs=out_specs, check_vma=False
    )
```
